256 devices in a mesh: replica: 16 (over y_lo, x, core), fsdp: 16 (over z, y_hi).
Axes of the slice: x: 4, y: 4 (y_hi: 2, y_lo: 2; y = y_hi * 2 + y_lo), z: 8, core: 2. Of those that a mesh axis runs over, the one named last changes fastest.
Arguments:
- activations: bfloat16 [65536, 8192], P(('replica', 'fsdp')), may hold values from -6 to 6
- cotangent: bfloat16 [65536, 512], P(('replica', 'fsdp')), may hold values from -12288 to 12288
- labels: int32 [65536], P(('replica', 'fsdp')), may hold values from -1 to 128255, as said below
- local_weight: float32 [16, 8192, 512], P('replica', 'fsdp'), may hold values from -4.5 to 4.5
- first_moment: bfloat16 [16, 8192, 512], P('replica', 'fsdp'), may hold values from -1.75 to 1.75
- second_moment: bfloat16 [16, 8192, 512], P('replica', 'fsdp'), may hold values from 0.019897461 to 2
- anchor_weight: float32 [8192, 512], P('fsdp'), may hold values from -4 to 4
- outer_state: float32 [8192, 512], P('fsdp'), may hold values from -1.75 to 1.75
Outputs:
- input_grad: bfloat16 [65536, 8192], P(('replica', 'fsdp'))
- new_anchor: float32 [8192, 512], P('fsdp')
- new_state: float32 [8192, 512], P('fsdp')
- new_first: bfloat16 [16, 8192, 512], P('replica', 'fsdp')
- new_second: bfloat16 [16, 8192, 512], P('replica', 'fsdp')
The draws below stay inside these ranges and needn't reach their ends.
Inputs may be any that keep to these rules, and one draw needn't show every extreme that they name: `labels`: each worker's tokens begin with a prompt of at least 512 tokens, labelled -1, and all later tokens carry ids of 0 to 128255; at least 512 of them do.
All inputs are finite; a program needn't handle non-finite values.
Results may differ from the reference program's by a relative error of at most 0.0059.
Values may be sent and summed in bfloat16 or wider, within the bound.
No kernel may reach another device: no remote copies, remote signals or barrier semaphores. Data moves between devices by JAX's collectives and lax.ppermute only.
A program may use at most 128 MiB of HBM per device.

```python
import math
import jax
import jax.numpy as jnp
from jax import lax

D = 8192
KV_WIDTH = 512
VOCAB = 128256
TOKENS = 4096
N_REPLICA = 16


def draw_labels(key, part):
    length = TOKENS
    starts = jax.random.randint(jax.random.fold_in(key, 3), (N_REPLICA, 1), length // 8, length - length // 8 + 1)
    target_ids = jax.random.randint(jax.random.fold_in(key, 5), (N_REPLICA, length), 0, VOCAB)
    position = lax.broadcasted_iota(jnp.int32, (N_REPLICA, length), 1)
    target_ids = jnp.where(position == length - 1, VOCAB - 1, target_ids)
    return jnp.where(position < starts, -1, target_ids).reshape(-1).astype(jnp.int32)


def common_weights(key):
    shared = jnp.clip(jax.random.normal(jax.random.fold_in(key, 17), (D, KV_WIDTH), jnp.float32), -4.0, 4.0)
    offset = 0.3 * jax.random.normal(jax.random.fold_in(key, 19), (N_REPLICA, D, KV_WIDTH), jnp.float32)
    local = jnp.clip(shared[None] + offset, -4.5, 4.5)
    return (shared, local)


def draw_anchor_weight(key, part):
    return common_weights(key)[0].astype(jnp.float32)


def draw_local_weight(key, part):
    return common_weights(key)[1].astype(jnp.float32)


def levels(key, extent, cuts, smallest, top_value):
    gain, own = 1.0, jax.random.fold_in(key, 6)
    for dim, blocks in cuts:
        steps = jnp.exp(jax.random.uniform(jax.random.fold_in(own, dim), (blocks,), jnp.float32, smallest / len(cuts), top_value / len(cuts)))
        gain = gain * jnp.repeat(steps, extent[dim] // blocks).reshape([-1 if axis == dim else 1 for axis in range(len(extent))])
    return gain


def scatter_about(rng, dims, width, limit, cuts=(), held_as=jnp.bfloat16):
    values = width * jax.random.normal(rng, dims, jnp.float32)
    if cuts:
        values = values * levels(rng, dims, cuts, -0.22, 0.18)
    return jnp.clip(values, -limit, limit).astype(held_as)


def setup_inputs(seed: int = 0) -> dict:
    arg_keys = jax.random.split(jax.random.key(seed), 9)
    activations = scatter_about(arg_keys[0], (N_REPLICA * TOKENS, D), 1.0, 6.0, ((0, 256),))
    cotangent = scatter_about(arg_keys[1], (N_REPLICA * TOKENS, KV_WIDTH), (TOKENS / 2), 12288.0, ((0, 256),))
    labels = draw_labels(jax.random.fold_in(arg_keys[8], 71), 0)
    local_weight = draw_local_weight(jax.random.fold_in(arg_keys[8], 71), 0)
    first_moment = scatter_about(arg_keys[4], (N_REPLICA, D, KV_WIDTH), 0.3, 1.75, ((0, 16), (1, 16)))
    second_moment = jnp.clip(jnp.exp(math.log(2.0) - 4.61031033 * jax.random.uniform(arg_keys[5], (N_REPLICA, D, KV_WIDTH), jnp.float32) ** levels(arg_keys[5], (N_REPLICA, D, KV_WIDTH), ((0, 16), (1, 16)), -0.2, 0.2)), 0.019897461, 2.0).astype(jnp.bfloat16)
    anchor_weight = draw_anchor_weight(jax.random.fold_in(arg_keys[8], 71), 0)
    outer_state = scatter_about(arg_keys[7], (D, KV_WIDTH), 0.3, 1.75, ((0, 16),), jnp.float32)
    return {"activations": activations, "cotangent": cotangent, "labels": labels, "local_weight": local_weight, "first_moment": first_moment, "second_moment": second_moment, "anchor_weight": anchor_weight, "outer_state": outer_state}


norm_eps = 1e-05
beta_first = 0.9
beta_second = 0.95
adam_eps = 1e-08
weight_decay = 0.1
inner_rate = 0.1
outer_rate = 0.7
outer_momentum = 0.9

def replica_step(operands):
    activations, cotangent, labels, local_weight, first_moment, second_moment, anchor_weight = operands
    width_scale = D ** (-0.5)
    values = activations.astype(jnp.float32)
    inverse = lax.rsqrt(lax.optimization_barrier(jnp.mean(values * values, axis=1, keepdims=True)) + norm_eps)
    normed = values * inverse
    normed_low = normed.astype(jnp.bfloat16)
    answer = (labels >= 0).astype(jnp.float32)
    answers = jnp.sum(answer)
    scaled = (cotangent.astype(jnp.float32) * answer[:, None] / answers).astype(jnp.bfloat16)
    gradient = width_scale * jnp.dot(normed_low.T, scaled, preferred_element_type=jnp.float32)
    weight_low = local_weight.astype(jnp.bfloat16)
    feature_grad = width_scale * jnp.dot(scaled, weight_low.T, preferred_element_type=jnp.float32)
    projected = lax.optimization_barrier(jnp.mean(feature_grad * normed, axis=1, keepdims=True))
    input_grad = (inverse * (feature_grad - normed * projected)).astype(jnp.bfloat16)
    first = beta_first * first_moment.astype(jnp.float32) + (1.0 - beta_first) * gradient
    second = beta_second * second_moment.astype(jnp.float32) + (1.0 - beta_second) * gradient * gradient
    stepped = local_weight - inner_rate * (first / (jnp.sqrt(second) + adam_eps) + weight_decay * local_weight)
    pseudo_grad = anchor_weight - stepped
    return (input_grad, first.astype(jnp.bfloat16), second.astype(jnp.bfloat16), pseudo_grad)

def reference(activations, cotangent, labels, local_weight, first_moment, second_moment, anchor_weight, outer_state):
    operands = (activations.reshape(N_REPLICA, TOKENS, D), cotangent.reshape(N_REPLICA, TOKENS, KV_WIDTH), labels.reshape(N_REPLICA, TOKENS), local_weight, first_moment, second_moment, jnp.broadcast_to(anchor_weight[None], local_weight.shape))
    input_grad, new_first, new_second, pseudo_grad = lax.map(replica_step, operands)
    average = lax.optimization_barrier(jnp.sum(pseudo_grad, axis=0)) / N_REPLICA
    new_state = outer_momentum * outer_state + average
    new_anchor = anchor_weight - outer_rate * (average + outer_momentum * new_state)
    return (input_grad.reshape(N_REPLICA * TOKENS, D), new_anchor, new_state, new_first, new_second)
```

```python
import jax
import jax.numpy as jnp
from jax import lax
from jax.sharding import PartitionSpec as P

D = 8192


norm_eps = 1e-05
beta_first = 0.9
beta_second = 0.95
adam_eps = 1e-08
weight_decay = 0.1
inner_rate = 0.1
outer_rate = 0.7
outer_momentum = 0.9


def contract_last(left, right):
    return lax.dot_general(
        left, right, (((1,), (1,)), ((), ())), preferred_element_type=jnp.float32
    )


def contract_first(left, right):
    return lax.dot_general(
        left, right, (((0,), (0,)), ((), ())), preferred_element_type=jnp.float32
    )


def per_device(
    activations,
    cotangent,
    labels,
    local_weight,
    first_moment,
    second_moment,
    anchor_weight,
    outer_state,
):
    width_scale = D ** (-0.5)
    weight_shard = local_weight[0]
    weight_low = weight_shard.astype(jnp.bfloat16)
    all_weight = lax.all_gather(weight_low, "fsdp", axis=0, tiled=True)
    all_labels = lax.all_gather(labels, "fsdp", axis=0, tiled=True)
    all_cotangent = lax.all_gather(cotangent, "fsdp", axis=0, tiled=True)
    answers = jnp.sum((all_labels >= 0).astype(jnp.float32))
    answer = (labels >= 0).astype(jnp.float32)
    all_answer = (all_labels >= 0).astype(jnp.float32)
    all_scaled = (
        all_cotangent.astype(jnp.float32) * all_answer[:, None] / answers
    ).astype(jnp.bfloat16)
    scaled = (cotangent.astype(jnp.float32) * answer[:, None] / answers).astype(jnp.bfloat16)
    values = activations.astype(jnp.float32)
    inverse = lax.rsqrt(jnp.mean(values * values, axis=1, keepdims=True) + norm_eps)
    normed = values * inverse
    normed_low = normed.astype(jnp.bfloat16)
    columns = lax.all_to_all(normed_low, "fsdp", 1, 0, tiled=True)
    gradient = width_scale * contract_first(columns, all_scaled)
    feature_grad = width_scale * contract_last(scaled, all_weight)
    projected = jnp.mean(feature_grad * normed, axis=1, keepdims=True)
    input_grad = (inverse * (feature_grad - normed * projected)).astype(jnp.bfloat16)
    first = beta_first * first_moment[0].astype(jnp.float32) + (1.0 - beta_first) * gradient
    second = (
        beta_second * second_moment[0].astype(jnp.float32)
        + (1.0 - beta_second) * gradient * gradient
    )
    stepped = weight_shard - inner_rate * (
        first / (jnp.sqrt(second) + adam_eps) + weight_decay * weight_shard
    )
    pseudo_grad = anchor_weight - stepped
    replicas = lax.axis_size("replica")
    average = lax.psum(pseudo_grad.astype(jnp.bfloat16), "replica").astype(jnp.float32) / replicas
    new_state = outer_momentum * outer_state + average
    new_anchor = anchor_weight - outer_rate * (average + outer_momentum * new_state)
    new_first = first.astype(jnp.bfloat16)[None]
    new_second = second.astype(jnp.bfloat16)[None]
    return (input_grad, new_anchor, new_state, new_first, new_second)


def solution(mesh):
    in_specs = (
        P(("replica", "fsdp"), None),
        P(("replica", "fsdp"), None),
        P(("replica", "fsdp")),
        P("replica", "fsdp", None),
        P("replica", "fsdp", None),
        P("replica", "fsdp", None),
        P("fsdp", None),
        P("fsdp", None),
    )
    out_specs = (
        P(("replica", "fsdp"), None),
        P("fsdp", None),
        P("fsdp", None),
        P("replica", "fsdp", None),
        P("replica", "fsdp", None),
    )
    return jax.shard_map(
        per_device, mesh=mesh, in_specs=in_specs, out_specs=out_specs, check_vma=False
    )
```

```python
import jax
import jax.numpy as jnp
from jax import lax
from jax.sharding import PartitionSpec as P

D = 8192


norm_eps = 1e-05
beta_first = 0.9
beta_second = 0.95
adam_eps = 1e-08
weight_decay = 0.1
inner_rate = 0.1
outer_rate = 0.7
outer_momentum = 0.9


def contract_last(left, right):
    return lax.dot_general(
        left, right, (((1,), (1,)), ((), ())), preferred_element_type=jnp.float32
    )


def contract_first(left, right):
    return lax.dot_general(
        left, right, (((0,), (0,)), ((), ())), preferred_element_type=jnp.float32
    )


def gather_rows(block, axis):
    count = lax.axis_size(axis)
    copies = jnp.broadcast_to(block[None], (count,) + block.shape)
    gathered = lax.all_to_all(copies, axis, 0, 0, tiled=True)
    return gathered.reshape((count * block.shape[0],) + block.shape[1:])


def sum_rows(block, axis):
    count = lax.axis_size(axis)
    pieces = block.reshape((count, block.shape[0] // count) + block.shape[1:])
    received = lax.all_to_all(pieces, axis, 0, 0, tiled=True)
    partial = jnp.sum(received.astype(jnp.float32), axis=0).astype(block.dtype)
    return gather_rows(partial, axis)


def per_device(
    activations,
    cotangent,
    labels,
    local_weight,
    first_moment,
    second_moment,
    anchor_weight,
    outer_state,
):
    width_scale = D ** (-0.5)
    weight_shard = local_weight[0]
    weight_low = weight_shard.astype(jnp.bfloat16)
    all_weight = gather_rows(weight_low, "fsdp")
    all_labels = gather_rows(labels, "fsdp")
    all_cotangent = gather_rows(cotangent, "fsdp")
    answers = jnp.sum((all_labels >= 0).astype(jnp.float32))
    answer = (labels >= 0).astype(jnp.float32)
    all_answer = (all_labels >= 0).astype(jnp.float32)
    all_scaled = (
        all_cotangent.astype(jnp.float32) * all_answer[:, None] / answers
    ).astype(jnp.bfloat16)
    scaled = (cotangent.astype(jnp.float32) * answer[:, None] / answers).astype(jnp.bfloat16)
    values = activations.astype(jnp.float32)
    inverse = lax.rsqrt(jnp.mean(values * values, axis=1, keepdims=True) + norm_eps)
    normed = values * inverse
    normed_low = normed.astype(jnp.bfloat16)
    columns = lax.all_to_all(normed_low, "fsdp", 1, 0, tiled=True)
    gradient = width_scale * contract_first(columns, all_scaled)
    feature_grad = width_scale * contract_last(scaled, all_weight)
    projected = jnp.mean(feature_grad * normed, axis=1, keepdims=True)
    input_grad = (inverse * (feature_grad - normed * projected)).astype(jnp.bfloat16)
    first = beta_first * first_moment[0].astype(jnp.float32) + (1.0 - beta_first) * gradient
    second = (
        beta_second * second_moment[0].astype(jnp.float32)
        + (1.0 - beta_second) * gradient * gradient
    )
    stepped = weight_shard - inner_rate * (
        first / (jnp.sqrt(second) + adam_eps) + weight_decay * weight_shard
    )
    pseudo_grad = anchor_weight - stepped
    replicas = lax.axis_size("replica")
    average = sum_rows(pseudo_grad.astype(jnp.bfloat16), "replica").astype(jnp.float32) / replicas
    new_state = outer_momentum * outer_state + average
    new_anchor = anchor_weight - outer_rate * (average + outer_momentum * new_state)
    new_first = first.astype(jnp.bfloat16)[None]
    new_second = second.astype(jnp.bfloat16)[None]
    return (input_grad, new_anchor, new_state, new_first, new_second)


def solution(mesh):
    in_specs = (
        P(("replica", "fsdp"), None),
        P(("replica", "fsdp"), None),
        P(("replica", "fsdp")),
        P("replica", "fsdp", None),
        P("replica", "fsdp", None),
        P("replica", "fsdp", None),
        P("fsdp", None),
        P("fsdp", None),
    )
    out_specs = (
        P(("replica", "fsdp"), None),
        P("fsdp", None),
        P("fsdp", None),
        P("replica", "fsdp", None),
        P("replica", "fsdp", None),
    )
    return jax.shard_map(
        per_device, mesh=mesh, in_specs=in_specs, out_specs=out_specs, check_vma=False
    )
```

```python
import jax
import jax.numpy as jnp
from jax import lax
from jax.sharding import PartitionSpec as P

D = 8192


norm_eps = 1e-05
beta_first = 0.9
beta_second = 0.95
adam_eps = 1e-08
weight_decay = 0.1
inner_rate = 0.1
outer_rate = 0.7
outer_momentum = 0.9


def contract_last(left, right):
    return lax.dot_general(
        left, right, (((1,), (1,)), ((), ())), preferred_element_type=jnp.float32
    )


def contract_first(left, right):
    return lax.dot_general(
        left, right, (((0,), (0,)), ((), ())), preferred_element_type=jnp.float32
    )


def gather_rows(block, axis):
    count = lax.axis_size(axis)
    copies = jnp.broadcast_to(block[None], (count,) + block.shape)
    gathered = lax.all_to_all(copies, axis, 0, 0, tiled=True)
    return gathered.reshape((count * block.shape[0],) + block.shape[1:])


def sum_rows(block, axis):
    count = lax.axis_size(axis)
    pieces = block.reshape((count, block.shape[0] // count) + block.shape[1:])
    received = lax.all_to_all(pieces, axis, 0, 0, tiled=True)
    partial = jnp.sum(received.astype(jnp.float32), axis=0).astype(block.dtype)
    return gather_rows(partial, axis)


def per_device(
    activations,
    cotangent,
    labels,
    local_weight,
    first_moment,
    second_moment,
    anchor_weight,
    outer_state,
):
    width_scale = D ** (-0.5)
    weight_shard = local_weight[0]
    weight_low = weight_shard.astype(jnp.bfloat16)
    answer = (labels >= 0).astype(jnp.float32)
    rows, width = weight_low.shape
    tokens = cotangent.shape[0]
    flags = jnp.zeros((16, width), jnp.bfloat16).at[0, :tokens].set(answer.astype(jnp.bfloat16))
    packed = jnp.concatenate([weight_low, cotangent, flags], axis=0)
    gathered = lax.all_gather(packed, "fsdp", axis=0, tiled=False)
    count = gathered.shape[0]
    all_weight = gathered[:, :rows].reshape(count * rows, width)
    all_cotangent = gathered[:, rows : rows + tokens].reshape(count * tokens, width)
    all_answer = gathered[:, rows + tokens, :tokens].reshape(count * tokens).astype(jnp.float32)
    answers = jnp.sum(all_answer)
    all_scaled = (
        all_cotangent.astype(jnp.float32) * all_answer[:, None] / answers
    ).astype(jnp.bfloat16)
    scaled = (cotangent.astype(jnp.float32) * answer[:, None] / answers).astype(jnp.bfloat16)
    values = activations.astype(jnp.float32)
    inverse = lax.rsqrt(jnp.mean(values * values, axis=1, keepdims=True) + norm_eps)
    normed = values * inverse
    normed_low = normed.astype(jnp.bfloat16)
    columns = lax.all_to_all(normed_low, "fsdp", 1, 0, tiled=True)
    gradient = width_scale * contract_first(columns, all_scaled)
    feature_grad = width_scale * contract_last(scaled, all_weight)
    projected = jnp.mean(feature_grad * normed, axis=1, keepdims=True)
    input_grad = (inverse * (feature_grad - normed * projected)).astype(jnp.bfloat16)
    first = beta_first * first_moment[0].astype(jnp.float32) + (1.0 - beta_first) * gradient
    second = (
        beta_second * second_moment[0].astype(jnp.float32)
        + (1.0 - beta_second) * gradient * gradient
    )
    stepped = weight_shard - inner_rate * (
        first / (jnp.sqrt(second) + adam_eps) + weight_decay * weight_shard
    )
    pseudo_grad = anchor_weight - stepped
    replicas = lax.axis_size("replica")
    average = sum_rows(pseudo_grad.astype(jnp.bfloat16), "replica").astype(jnp.float32) / replicas
    new_state = outer_momentum * outer_state + average
    new_anchor = anchor_weight - outer_rate * (average + outer_momentum * new_state)
    new_first = first.astype(jnp.bfloat16)[None]
    new_second = second.astype(jnp.bfloat16)[None]
    return (input_grad, new_anchor, new_state, new_first, new_second)


def solution(mesh):
    in_specs = (
        P(("replica", "fsdp"), None),
        P(("replica", "fsdp"), None),
        P(("replica", "fsdp")),
        P("replica", "fsdp", None),
        P("replica", "fsdp", None),
        P("replica", "fsdp", None),
        P("fsdp", None),
        P("fsdp", None),
    )
    out_specs = (
        P(("replica", "fsdp"), None),
        P("fsdp", None),
        P("fsdp", None),
        P("replica", "fsdp", None),
        P("replica", "fsdp", None),
    )
    return jax.shard_map(
        per_device, mesh=mesh, in_specs=in_specs, out_specs=out_specs, check_vma=False
    )
```

```python
import jax
import jax.numpy as jnp
from jax import lax
from jax.sharding import PartitionSpec as P

D = 8192


norm_eps = 1e-05
beta_first = 0.9
beta_second = 0.95
adam_eps = 1e-08
weight_decay = 0.1
inner_rate = 0.1
outer_rate = 0.7
outer_momentum = 0.9


def contract_last(left, right):
    return lax.dot_general(
        left, right, (((1,), (1,)), ((), ())), preferred_element_type=jnp.float32
    )


def contract_first(left, right):
    return lax.dot_general(
        left, right, (((0,), (0,)), ((), ())), preferred_element_type=jnp.float32
    )


def gather_rows(block, axis):
    count = lax.axis_size(axis)
    copies = jnp.broadcast_to(block[None], (count,) + block.shape)
    gathered = lax.all_to_all(copies, axis, 0, 0, tiled=True)
    return gathered.reshape((count * block.shape[0],) + block.shape[1:])


def sum_rows(block, axis):
    count = lax.axis_size(axis)
    pieces = block.reshape((count, block.shape[0] // count) + block.shape[1:])
    received = lax.all_to_all(pieces, axis, 0, 0, tiled=True)
    partial = jnp.sum(received.astype(jnp.float32), axis=0).astype(block.dtype)
    return gather_rows(partial, axis)


def per_device(
    activations,
    cotangent,
    labels,
    local_weight,
    first_moment,
    second_moment,
    anchor_weight,
    outer_state,
):
    width_scale = D ** (-0.5)
    weight_shard = local_weight[0]
    weight_low = weight_shard.astype(jnp.bfloat16)
    answer = (labels >= 0).astype(jnp.float32)
    rows, width = weight_low.shape
    tokens = cotangent.shape[0]
    flags = jnp.zeros((16, width), jnp.bfloat16).at[0, :tokens].set(answer.astype(jnp.bfloat16))
    packed = jnp.concatenate([weight_low, cotangent, flags], axis=0)
    gathered = lax.all_gather(packed, "fsdp", axis=0, tiled=False)
    values = activations.astype(jnp.float32)
    inverse = lax.rsqrt(jnp.mean(values * values, axis=1, keepdims=True) + norm_eps)
    normed = values * inverse
    normed_low = normed.astype(jnp.bfloat16)
    columns = lax.all_to_all(normed_low, "fsdp", 1, 0, tiled=True)
    gathered, columns = lax.optimization_barrier((gathered, columns))
    count = gathered.shape[0]
    all_weight = gathered[:, :rows].reshape(count * rows, width)
    all_cotangent = gathered[:, rows : rows + tokens].reshape(count * tokens, width)
    all_answer = gathered[:, rows + tokens, :tokens].reshape(count * tokens).astype(jnp.float32)
    answers = jnp.sum(all_answer)
    all_scaled = (
        all_cotangent.astype(jnp.float32) * all_answer[:, None] / answers
    ).astype(jnp.bfloat16)
    scaled = (cotangent.astype(jnp.float32) * answer[:, None] / answers).astype(jnp.bfloat16)
    gradient = width_scale * contract_first(columns, all_scaled)
    feature_grad = width_scale * contract_last(scaled, all_weight)
    projected = jnp.mean(feature_grad * normed, axis=1, keepdims=True)
    input_grad = (inverse * (feature_grad - normed * projected)).astype(jnp.bfloat16)
    first = beta_first * first_moment[0].astype(jnp.float32) + (1.0 - beta_first) * gradient
    second = (
        beta_second * second_moment[0].astype(jnp.float32)
        + (1.0 - beta_second) * gradient * gradient
    )
    stepped = weight_shard - inner_rate * (
        first / (jnp.sqrt(second) + adam_eps) + weight_decay * weight_shard
    )
    pseudo_grad = anchor_weight - stepped
    replicas = lax.axis_size("replica")
    average = sum_rows(pseudo_grad.astype(jnp.bfloat16), "replica").astype(jnp.float32) / replicas
    new_state = outer_momentum * outer_state + average
    new_anchor = anchor_weight - outer_rate * (average + outer_momentum * new_state)
    new_first = first.astype(jnp.bfloat16)[None]
    new_second = second.astype(jnp.bfloat16)[None]
    return (input_grad, new_anchor, new_state, new_first, new_second)


def solution(mesh):
    in_specs = (
        P(("replica", "fsdp"), None),
        P(("replica", "fsdp"), None),
        P(("replica", "fsdp")),
        P("replica", "fsdp", None),
        P("replica", "fsdp", None),
        P("replica", "fsdp", None),
        P("fsdp", None),
        P("fsdp", None),
    )
    out_specs = (
        P(("replica", "fsdp"), None),
        P("fsdp", None),
        P("fsdp", None),
        P("replica", "fsdp", None),
        P("replica", "fsdp", None),
    )
    return jax.shard_map(
        per_device, mesh=mesh, in_specs=in_specs, out_specs=out_specs, check_vma=False
    )
```

```python
import jax
import jax.numpy as jnp
from jax import lax
from jax.sharding import PartitionSpec as P

D = 8192


norm_eps = 1e-05
beta_first = 0.9
beta_second = 0.95
adam_eps = 1e-08
weight_decay = 0.1
inner_rate = 0.1
outer_rate = 0.7
outer_momentum = 0.9


def contract_last(left, right):
    return lax.dot_general(
        left, right, (((1,), (1,)), ((), ())), preferred_element_type=jnp.float32
    )


def contract_first(left, right):
    return lax.dot_general(
        left, right, (((0,), (0,)), ((), ())), preferred_element_type=jnp.float32
    )


def gather_rows(block, axis):
    count = lax.axis_size(axis)
    copies = jnp.broadcast_to(block[None], (count,) + block.shape)
    gathered = lax.all_to_all(copies, axis, 0, 0, tiled=True)
    return gathered.reshape((count * block.shape[0],) + block.shape[1:])


def sum_rows(block, axis):
    count = lax.axis_size(axis)
    pieces = block.reshape((count, block.shape[0] // count) + block.shape[1:])
    received = lax.all_to_all(pieces, axis, 0, 0, tiled=True)
    partial = jnp.sum(received.astype(jnp.float32), axis=0).astype(block.dtype)
    return gather_rows(partial, axis)


def ring_sum_rows(partial, axis):
    count = lax.axis_size(axis)
    stations = count // 2
    me = lax.axis_index(axis)
    station = me // 2
    side = me % 2
    total, width = partial.shape
    group = total // stations
    half = width // 2
    blocks = partial.reshape(stations, group, width)
    ahead = [(i, ((i // 2 + 1) % stations) * 2 + i % 2) for i in range(count)]
    behind = [(i, ((i // 2 - 1) % stations) * 2 + i % 2) for i in range(count)]

    def block(index):
        return lax.dynamic_index_in_dim(blocks, index % stations, 0, keepdims=False)

    forward = block(station - 1)[:, :half]
    backward = block(station + 1)[:, half:]
    for step in range(stations - 1):
        forward = lax.ppermute(forward.astype(jnp.bfloat16), axis, ahead).astype(jnp.float32)
        backward = lax.ppermute(backward.astype(jnp.bfloat16), axis, behind).astype(jnp.float32)
        forward = forward + block(station - step - 2)[:, :half]
        backward = backward + block(station + step + 2)[:, half:]
    combined = jnp.concatenate([forward, backward], axis=1)
    rows = group // 2
    mine = lax.dynamic_slice_in_dim(combined, side * rows, rows, 0)
    theirs = lax.dynamic_slice_in_dim(combined, (1 - side) * rows, rows, 0)
    partner = [(i, i ^ 1) for i in range(count)]
    received = lax.ppermute(theirs.astype(jnp.bfloat16), axis, partner).astype(jnp.float32)
    return mine + received


def per_device(
    activations,
    cotangent,
    labels,
    local_weight,
    first_moment,
    second_moment,
    anchor_weight,
    outer_state,
):
    width_scale = D ** (-0.5)
    weight_shard = local_weight[0]
    weight_low = weight_shard.astype(jnp.bfloat16)
    answer = (labels >= 0).astype(jnp.float32)
    rows, width = weight_low.shape
    tokens = cotangent.shape[0]
    flags = jnp.zeros((16, width), jnp.bfloat16).at[0, :tokens].set(answer.astype(jnp.bfloat16))
    packed = jnp.concatenate([weight_low, flags], axis=0)
    gathered = lax.all_gather(packed, "fsdp", axis=0, tiled=False)
    values = activations.astype(jnp.float32)
    inverse = lax.rsqrt(jnp.mean(values * values, axis=1, keepdims=True) + norm_eps)
    normed = values * inverse
    normed_low = normed.astype(jnp.bfloat16)
    kept = (cotangent.astype(jnp.float32) * answer[:, None]).astype(jnp.bfloat16)
    reduced = ring_sum_rows(contract_first(normed_low, kept), "fsdp")
    gathered, reduced = lax.optimization_barrier((gathered, reduced))
    count = gathered.shape[0]
    all_weight = gathered[:, :rows].reshape(count * rows, width)
    all_answer = gathered[:, rows, :tokens].reshape(count * tokens).astype(jnp.float32)
    answers = jnp.sum(all_answer)
    scaled = (cotangent.astype(jnp.float32) * answer[:, None] / answers).astype(jnp.bfloat16)
    gradient = width_scale * reduced / answers
    feature_grad = width_scale * contract_last(scaled, all_weight)
    projected = jnp.mean(feature_grad * normed, axis=1, keepdims=True)
    input_grad = (inverse * (feature_grad - normed * projected)).astype(jnp.bfloat16)
    first = beta_first * first_moment[0].astype(jnp.float32) + (1.0 - beta_first) * gradient
    second = (
        beta_second * second_moment[0].astype(jnp.float32)
        + (1.0 - beta_second) * gradient * gradient
    )
    stepped = weight_shard - inner_rate * (
        first / (jnp.sqrt(second) + adam_eps) + weight_decay * weight_shard
    )
    pseudo_grad = anchor_weight - stepped
    replicas = lax.axis_size("replica")
    average = sum_rows(pseudo_grad.astype(jnp.bfloat16), "replica").astype(jnp.float32) / replicas
    new_state = outer_momentum * outer_state + average
    new_anchor = anchor_weight - outer_rate * (average + outer_momentum * new_state)
    new_first = first.astype(jnp.bfloat16)[None]
    new_second = second.astype(jnp.bfloat16)[None]
    return (input_grad, new_anchor, new_state, new_first, new_second)


def solution(mesh):
    in_specs = (
        P(("replica", "fsdp"), None),
        P(("replica", "fsdp"), None),
        P(("replica", "fsdp")),
        P("replica", "fsdp", None),
        P("replica", "fsdp", None),
        P("replica", "fsdp", None),
        P("fsdp", None),
        P("fsdp", None),
    )
    out_specs = (
        P(("replica", "fsdp"), None),
        P("fsdp", None),
        P("fsdp", None),
        P("replica", "fsdp", None),
        P("replica", "fsdp", None),
    )
    return jax.shard_map(
        per_device, mesh=mesh, in_specs=in_specs, out_specs=out_specs, check_vma=False
    )
```

```python
import jax
import jax.numpy as jnp
from jax import lax
from jax.sharding import PartitionSpec as P

D = 8192


norm_eps = 1e-05
beta_first = 0.9
beta_second = 0.95
adam_eps = 1e-08
weight_decay = 0.1
inner_rate = 0.1
outer_rate = 0.7
outer_momentum = 0.9


def contract_last(left, right):
    return lax.dot_general(
        left, right, (((1,), (1,)), ((), ())), preferred_element_type=jnp.float32
    )


def contract_first(left, right):
    return lax.dot_general(
        left, right, (((0,), (0,)), ((), ())), preferred_element_type=jnp.float32
    )


def gather_rows(block, axis):
    count = lax.axis_size(axis)
    copies = jnp.broadcast_to(block[None], (count,) + block.shape)
    gathered = lax.all_to_all(copies, axis, 0, 0, tiled=True)
    return gathered.reshape((count * block.shape[0],) + block.shape[1:])


def sum_rows(block, axis):
    count = lax.axis_size(axis)
    pieces = block.reshape((count, block.shape[0] // count) + block.shape[1:])
    received = lax.all_to_all(pieces, axis, 0, 0, tiled=True)
    partial = jnp.sum(received.astype(jnp.float32), axis=0).astype(block.dtype)
    return gather_rows(partial, axis)


def ring_sum_rows(normed_low, kept, axis):
    count = lax.axis_size(axis)
    stations = count // 2
    me = lax.axis_index(axis)
    station = me // 2
    side = me % 2
    features = normed_low.shape[1]
    width = kept.shape[1]
    group = features // stations
    half = width // 2
    ahead = [(i, ((i // 2 + 1) % stations) * 2 + i % 2) for i in range(count)]
    behind = [(i, ((i // 2 - 1) % stations) * 2 + i % 2) for i in range(count)]
    kept_forward = kept[:, :half]
    kept_backward = kept[:, half:]

    def block(index, right):
        start = pl_multiple((index % stations) * group, group)
        piece = lax.dynamic_slice_in_dim(normed_low, start, group, 1)
        return contract_first(piece, right)

    forward = block(station - 1, kept_forward)
    backward = block(station + 1, kept_backward)
    for step in range(stations - 1):
        forward = lax.ppermute(forward.astype(jnp.bfloat16), axis, ahead).astype(jnp.float32)
        backward = lax.ppermute(backward.astype(jnp.bfloat16), axis, behind).astype(jnp.float32)
        forward = forward + block(station - step - 2, kept_forward)
        backward = backward + block(station + step + 2, kept_backward)
    combined = jnp.concatenate([forward, backward], axis=1)
    rows = group // 2
    mine = lax.dynamic_slice_in_dim(combined, side * rows, rows, 0)
    theirs = lax.dynamic_slice_in_dim(combined, (1 - side) * rows, rows, 0)
    partner = [(i, i ^ 1) for i in range(count)]
    received = lax.ppermute(theirs.astype(jnp.bfloat16), axis, partner).astype(jnp.float32)
    return mine + received


def pl_multiple(value, step):
    return (value // step) * step


def per_device(
    activations,
    cotangent,
    labels,
    local_weight,
    first_moment,
    second_moment,
    anchor_weight,
    outer_state,
):
    width_scale = D ** (-0.5)
    weight_shard = local_weight[0]
    weight_low = weight_shard.astype(jnp.bfloat16)
    answer = (labels >= 0).astype(jnp.float32)
    rows, width = weight_low.shape
    tokens = cotangent.shape[0]
    flags = jnp.zeros((16, width), jnp.bfloat16).at[0, :tokens].set(answer.astype(jnp.bfloat16))
    packed = jnp.concatenate([weight_low, flags], axis=0)
    gathered = lax.all_gather(packed, "fsdp", axis=0, tiled=False)
    values = activations.astype(jnp.float32)
    inverse = lax.rsqrt(jnp.mean(values * values, axis=1, keepdims=True) + norm_eps)
    normed = values * inverse
    normed_low = normed.astype(jnp.bfloat16)
    kept = (cotangent.astype(jnp.float32) * answer[:, None]).astype(jnp.bfloat16)
    reduced = ring_sum_rows(normed_low, kept, "fsdp")
    gathered, reduced = lax.optimization_barrier((gathered, reduced))
    count = gathered.shape[0]
    all_weight = gathered[:, :rows].reshape(count * rows, width)
    all_answer = gathered[:, rows, :tokens].reshape(count * tokens).astype(jnp.float32)
    answers = jnp.sum(all_answer)
    scaled = (cotangent.astype(jnp.float32) * answer[:, None] / answers).astype(jnp.bfloat16)
    gradient = width_scale * reduced / answers
    feature_grad = width_scale * contract_last(scaled, all_weight)
    projected = jnp.mean(feature_grad * normed, axis=1, keepdims=True)
    input_grad = (inverse * (feature_grad - normed * projected)).astype(jnp.bfloat16)
    first = beta_first * first_moment[0].astype(jnp.float32) + (1.0 - beta_first) * gradient
    second = (
        beta_second * second_moment[0].astype(jnp.float32)
        + (1.0 - beta_second) * gradient * gradient
    )
    stepped = weight_shard - inner_rate * (
        first / (jnp.sqrt(second) + adam_eps) + weight_decay * weight_shard
    )
    pseudo_grad = anchor_weight - stepped
    replicas = lax.axis_size("replica")
    average = sum_rows(pseudo_grad.astype(jnp.bfloat16), "replica").astype(jnp.float32) / replicas
    new_state = outer_momentum * outer_state + average
    new_anchor = anchor_weight - outer_rate * (average + outer_momentum * new_state)
    new_first = first.astype(jnp.bfloat16)[None]
    new_second = second.astype(jnp.bfloat16)[None]
    return (input_grad, new_anchor, new_state, new_first, new_second)


def solution(mesh):
    in_specs = (
        P(("replica", "fsdp"), None),
        P(("replica", "fsdp"), None),
        P(("replica", "fsdp")),
        P("replica", "fsdp", None),
        P("replica", "fsdp", None),
        P("replica", "fsdp", None),
        P("fsdp", None),
        P("fsdp", None),
    )
    out_specs = (
        P(("replica", "fsdp"), None),
        P("fsdp", None),
        P("fsdp", None),
        P("replica", "fsdp", None),
        P("replica", "fsdp", None),
    )
    return jax.shard_map(
        per_device, mesh=mesh, in_specs=in_specs, out_specs=out_specs, check_vma=False
    )
```

```python
import jax
import jax.numpy as jnp
from jax import lax
from jax.sharding import PartitionSpec as P

D = 8192


norm_eps = 1e-05
beta_first = 0.9
beta_second = 0.95
adam_eps = 1e-08
weight_decay = 0.1
inner_rate = 0.1
outer_rate = 0.7
outer_momentum = 0.9


def contract_last(left, right):
    return lax.dot_general(
        left, right, (((1,), (1,)), ((), ())), preferred_element_type=jnp.float32
    )


def contract_first(left, right):
    return lax.dot_general(
        left, right, (((0,), (0,)), ((), ())), preferred_element_type=jnp.float32
    )


def gather_rows(block, axis):
    count = lax.axis_size(axis)
    copies = jnp.broadcast_to(block[None], (count,) + block.shape)
    gathered = lax.all_to_all(copies, axis, 0, 0, tiled=True)
    return gathered.reshape((count * block.shape[0],) + block.shape[1:])


def sum_rows(block, axis):
    count = lax.axis_size(axis)
    pieces = block.reshape((count, block.shape[0] // count) + block.shape[1:])
    received = lax.all_to_all(pieces, axis, 0, 0, tiled=True)
    partial = jnp.sum(received.astype(jnp.float32), axis=0).astype(block.dtype)
    return gather_rows(partial, axis)


def ring_sum_rows(normed_low, kept, axis):
    count = lax.axis_size(axis)
    stations = count // 2
    me = lax.axis_index(axis)
    station = me // 2
    side = me % 2
    features = normed_low.shape[1]
    width = kept.shape[1]
    group = features // stations
    half = width // 2
    ahead = [(i, ((i // 2 + 1) % stations) * 2 + i % 2) for i in range(count)]
    behind = [(i, ((i // 2 - 1) % stations) * 2 + i % 2) for i in range(count)]
    kept_forward = kept[:, :half]
    kept_backward = kept[:, half:]

    def block(index, right):
        start = pl_multiple((index % stations) * group, group)
        piece = lax.dynamic_slice_in_dim(normed_low, start, group, 1)
        return contract_first(piece, right)

    forward = block(station - 1, kept_forward)
    backward = block(station + 1, kept_backward)
    for step in range(stations - 1):
        forward = lax.ppermute(forward.astype(jnp.bfloat16), axis, ahead).astype(jnp.float32)
        backward = lax.ppermute(backward.astype(jnp.bfloat16), axis, behind).astype(jnp.float32)
        forward = forward + block(station - step - 2, kept_forward)
        backward = backward + block(station + step + 2, kept_backward)
    return jnp.concatenate([forward, backward], axis=1)


def pair_sum_rows(combined, axis):
    count = lax.axis_size(axis)
    side = lax.axis_index(axis) % 2
    rows = combined.shape[0] // 2
    mine = lax.dynamic_slice_in_dim(combined, side * rows, rows, 0)
    theirs = lax.dynamic_slice_in_dim(combined, (1 - side) * rows, rows, 0)
    partner = [(i, i ^ 1) for i in range(count)]
    received = lax.ppermute(theirs.astype(jnp.bfloat16), axis, partner).astype(jnp.float32)
    return mine + received


def pl_multiple(value, step):
    return (value // step) * step


def per_device(
    activations,
    cotangent,
    labels,
    local_weight,
    first_moment,
    second_moment,
    anchor_weight,
    outer_state,
):
    width_scale = D ** (-0.5)
    weight_shard = local_weight[0]
    weight_low = weight_shard.astype(jnp.bfloat16)
    answer = (labels >= 0).astype(jnp.float32)
    rows, width = weight_low.shape
    tokens = cotangent.shape[0]
    flags = jnp.zeros((16, width), jnp.bfloat16).at[0, :tokens].set(answer.astype(jnp.bfloat16))
    packed = jnp.concatenate([weight_low, flags], axis=0)
    gathered = lax.all_gather(packed, "fsdp", axis=0, tiled=False)
    values = activations.astype(jnp.float32)
    inverse = lax.rsqrt(jnp.mean(values * values, axis=1, keepdims=True) + norm_eps)
    normed = values * inverse
    normed_low = normed.astype(jnp.bfloat16)
    kept = (cotangent.astype(jnp.float32) * answer[:, None]).astype(jnp.bfloat16)
    combined = ring_sum_rows(normed_low, kept, "fsdp")
    gathered, combined = lax.optimization_barrier((gathered, combined))
    reduced = pair_sum_rows(combined, "fsdp")
    count = gathered.shape[0]
    all_weight = gathered[:, :rows].reshape(count * rows, width)
    all_answer = gathered[:, rows, :tokens].reshape(count * tokens).astype(jnp.float32)
    answers = jnp.sum(all_answer)
    scaled = (cotangent.astype(jnp.float32) * answer[:, None] / answers).astype(jnp.bfloat16)
    gradient = width_scale * reduced / answers
    feature_grad = width_scale * contract_last(scaled, all_weight)
    projected = jnp.mean(feature_grad * normed, axis=1, keepdims=True)
    input_grad = (inverse * (feature_grad - normed * projected)).astype(jnp.bfloat16)
    first = beta_first * first_moment[0].astype(jnp.float32) + (1.0 - beta_first) * gradient
    second = (
        beta_second * second_moment[0].astype(jnp.float32)
        + (1.0 - beta_second) * gradient * gradient
    )
    stepped = weight_shard - inner_rate * (
        first / (jnp.sqrt(second) + adam_eps) + weight_decay * weight_shard
    )
    pseudo_grad = anchor_weight - stepped
    replicas = lax.axis_size("replica")
    average = sum_rows(pseudo_grad.astype(jnp.bfloat16), "replica").astype(jnp.float32) / replicas
    new_state = outer_momentum * outer_state + average
    new_anchor = anchor_weight - outer_rate * (average + outer_momentum * new_state)
    new_first = first.astype(jnp.bfloat16)[None]
    new_second = second.astype(jnp.bfloat16)[None]
    return (input_grad, new_anchor, new_state, new_first, new_second)


def solution(mesh):
    in_specs = (
        P(("replica", "fsdp"), None),
        P(("replica", "fsdp"), None),
        P(("replica", "fsdp")),
        P("replica", "fsdp", None),
        P("replica", "fsdp", None),
        P("replica", "fsdp", None),
        P("fsdp", None),
        P("fsdp", None),
    )
    out_specs = (
        P(("replica", "fsdp"), None),
        P("fsdp", None),
        P("fsdp", None),
        P("replica", "fsdp", None),
        P("replica", "fsdp", None),
    )
    return jax.shard_map(
        per_device, mesh=mesh, in_specs=in_specs, out_specs=out_specs, check_vma=False
    )
```

```python
import jax
import jax.numpy as jnp
from jax import lax
from jax.experimental import pallas as pl
from jax.experimental.pallas import tpu as pltpu
from jax.sharding import PartitionSpec as P

D = 8192


norm_eps = 1e-05
beta_first = 0.9
beta_second = 0.95
adam_eps = 1e-08
weight_decay = 0.1
inner_rate = 0.1
outer_rate = 0.7
outer_momentum = 0.9


def contract_last(left, right):
    return lax.dot_general(
        left, right, (((1,), (1,)), ((), ())), preferred_element_type=jnp.float32
    )


def contract_first(left, right):
    return lax.dot_general(
        left, right, (((0,), (0,)), ((), ())), preferred_element_type=jnp.float32
    )


def gather_rows(block, axis):
    count = lax.axis_size(axis)
    copies = jnp.broadcast_to(block[None], (count,) + block.shape)
    gathered = lax.all_to_all(copies, axis, 0, 0, tiled=True)
    return gathered.reshape((count * block.shape[0],) + block.shape[1:])


def sum_rows(block, axis):
    count = lax.axis_size(axis)
    pieces = block.reshape((count, block.shape[0] // count) + block.shape[1:])
    received = lax.all_to_all(pieces, axis, 0, 0, tiled=True)
    partial = jnp.sum(received.astype(jnp.float32), axis=0).astype(block.dtype)
    return gather_rows(partial, axis)


def input_grad_kernel(scaled_ref, gathered_ref, act_ref, inv_ref, out_ref, feature_ref):
    chunks = gathered_ref.shape[0]
    rows = out_ref.shape[1] // chunks
    scaled = scaled_ref[...]
    inverse = inv_ref[...]
    total = jnp.zeros(inverse.shape, jnp.float32)
    for chunk in range(chunks):
        cols = slice(chunk * rows, (chunk + 1) * rows)
        weight = gathered_ref[chunk, :rows, :]
        feature = D ** (-0.5) * lax.dot_general(
            scaled, weight, (((1,), (1,)), ((), ())), preferred_element_type=jnp.float32
        )
        feature_ref[:, cols] = feature
        normed = act_ref[:, cols].astype(jnp.float32) * inverse
        total = total + jnp.sum(feature * normed, axis=1, keepdims=True)
    projected = total / out_ref.shape[1]
    for chunk in range(chunks):
        cols = slice(chunk * rows, (chunk + 1) * rows)
        normed = act_ref[:, cols].astype(jnp.float32) * inverse
        out_ref[:, cols] = (inverse * (feature_ref[:, cols] - normed * projected)).astype(out_ref.dtype)


def input_grad_of(scaled, gathered, activations, inverse):
    tokens, features = activations.shape
    vmem = pl.BlockSpec(memory_space=pltpu.VMEM)
    return pl.pallas_call(
        input_grad_kernel,
        out_shape=jax.ShapeDtypeStruct((tokens, features), jnp.bfloat16),
        in_specs=[vmem, vmem, vmem, vmem],
        out_specs=vmem,
        scratch_shapes=[pltpu.VMEM((tokens, features), jnp.float32)],
        compiler_params=pltpu.CompilerParams(vmem_limit_bytes=48 * 1024 * 1024),
        cost_estimate=pl.CostEstimate(
            flops=2 * tokens * features * scaled.shape[1],
            bytes_accessed=gathered.size * 2 + activations.size * 4 + scaled.size * 2,
            transcendentals=0,
        ),
    )(scaled, gathered, activations, inverse)


def ring_sum_rows(normed_low, kept, axis):
    count = lax.axis_size(axis)
    stations = count // 2
    me = lax.axis_index(axis)
    station = me // 2
    side = me % 2
    features = normed_low.shape[1]
    width = kept.shape[1]
    group = features // stations
    half = width // 2
    ahead = [(i, ((i // 2 + 1) % stations) * 2 + i % 2) for i in range(count)]
    behind = [(i, ((i // 2 - 1) % stations) * 2 + i % 2) for i in range(count)]
    kept_forward = kept[:, :half]
    kept_backward = kept[:, half:]

    def block(index, right):
        start = pl_multiple((index % stations) * group, group)
        piece = lax.dynamic_slice_in_dim(normed_low, start, group, 1)
        return contract_first(piece, right)

    forward = block(station - 1, kept_forward)
    backward = block(station + 1, kept_backward)
    for step in range(stations - 1):
        forward = lax.ppermute(forward.astype(jnp.bfloat16), axis, ahead).astype(jnp.float32)
        backward = lax.ppermute(backward.astype(jnp.bfloat16), axis, behind).astype(jnp.float32)
        forward = forward + block(station - step - 2, kept_forward)
        backward = backward + block(station + step + 2, kept_backward)
    return jnp.concatenate([forward, backward], axis=1)


def pair_sum_rows(combined, axis):
    count = lax.axis_size(axis)
    side = lax.axis_index(axis) % 2
    rows = combined.shape[0] // 2
    mine = lax.dynamic_slice_in_dim(combined, side * rows, rows, 0)
    theirs = lax.dynamic_slice_in_dim(combined, (1 - side) * rows, rows, 0)
    partner = [(i, i ^ 1) for i in range(count)]
    received = lax.ppermute(theirs.astype(jnp.bfloat16), axis, partner).astype(jnp.float32)
    return mine + received


def pl_multiple(value, step):
    return (value // step) * step


def per_device(
    activations,
    cotangent,
    labels,
    local_weight,
    first_moment,
    second_moment,
    anchor_weight,
    outer_state,
):
    width_scale = D ** (-0.5)
    weight_shard = local_weight[0]
    weight_low = weight_shard.astype(jnp.bfloat16)
    answer = (labels >= 0).astype(jnp.float32)
    rows, width = weight_low.shape
    tokens = cotangent.shape[0]
    flags = jnp.zeros((16, width), jnp.bfloat16).at[0, :tokens].set(answer.astype(jnp.bfloat16))
    packed = jnp.concatenate([weight_low, flags], axis=0)
    gathered = lax.all_gather(packed, "fsdp", axis=0, tiled=False)
    values = activations.astype(jnp.float32)
    inverse = lax.rsqrt(jnp.mean(values * values, axis=1, keepdims=True) + norm_eps)
    normed = values * inverse
    normed_low = normed.astype(jnp.bfloat16)
    kept = (cotangent.astype(jnp.float32) * answer[:, None]).astype(jnp.bfloat16)
    combined = ring_sum_rows(normed_low, kept, "fsdp")
    gathered, combined = lax.optimization_barrier((gathered, combined))
    reduced = pair_sum_rows(combined, "fsdp")
    count = gathered.shape[0]
    all_answer = gathered[:, rows, :tokens].reshape(count * tokens).astype(jnp.float32)
    answers = jnp.sum(all_answer)
    scaled = (cotangent.astype(jnp.float32) * answer[:, None] / answers).astype(jnp.bfloat16)
    gradient = width_scale * reduced / answers
    input_grad = input_grad_of(scaled, gathered, activations, inverse)
    first = beta_first * first_moment[0].astype(jnp.float32) + (1.0 - beta_first) * gradient
    second = (
        beta_second * second_moment[0].astype(jnp.float32)
        + (1.0 - beta_second) * gradient * gradient
    )
    stepped = weight_shard - inner_rate * (
        first / (jnp.sqrt(second) + adam_eps) + weight_decay * weight_shard
    )
    pseudo_grad = anchor_weight - stepped
    replicas = lax.axis_size("replica")
    average = sum_rows(pseudo_grad.astype(jnp.bfloat16), "replica").astype(jnp.float32) / replicas
    new_state = outer_momentum * outer_state + average
    new_anchor = anchor_weight - outer_rate * (average + outer_momentum * new_state)
    new_first = first.astype(jnp.bfloat16)[None]
    new_second = second.astype(jnp.bfloat16)[None]
    return (input_grad, new_anchor, new_state, new_first, new_second)


def solution(mesh):
    in_specs = (
        P(("replica", "fsdp"), None),
        P(("replica", "fsdp"), None),
        P(("replica", "fsdp")),
        P("replica", "fsdp", None),
        P("replica", "fsdp", None),
        P("replica", "fsdp", None),
        P("fsdp", None),
        P("fsdp", None),
    )
    out_specs = (
        P(("replica", "fsdp"), None),
        P("fsdp", None),
        P("fsdp", None),
        P("replica", "fsdp", None),
        P("replica", "fsdp", None),
    )
    return jax.shard_map(
        per_device, mesh=mesh, in_specs=in_specs, out_specs=out_specs, check_vma=False
    )
```

```python
import jax
import jax.numpy as jnp
from jax import lax
from jax.experimental import pallas as pl
from jax.experimental.pallas import tpu as pltpu
from jax.sharding import PartitionSpec as P

D = 8192


norm_eps = 1e-05
beta_first = 0.9
beta_second = 0.95
adam_eps = 1e-08
weight_decay = 0.1
inner_rate = 0.1
outer_rate = 0.7
outer_momentum = 0.9


def contract_last(left, right):
    return lax.dot_general(
        left, right, (((1,), (1,)), ((), ())), preferred_element_type=jnp.float32
    )


def contract_first(left, right):
    return lax.dot_general(
        left, right, (((0,), (0,)), ((), ())), preferred_element_type=jnp.float32
    )


def gather_rows(block, axis):
    count = lax.axis_size(axis)
    copies = jnp.broadcast_to(block[None], (count,) + block.shape)
    gathered = lax.all_to_all(copies, axis, 0, 0, tiled=True)
    return gathered.reshape((count * block.shape[0],) + block.shape[1:])


def sum_rows(block, axis):
    count = lax.axis_size(axis)
    pieces = block.reshape((count, block.shape[0] // count) + block.shape[1:])
    received = lax.all_to_all(pieces, axis, 0, 0, tiled=True)
    partial = jnp.sum(received.astype(jnp.float32), axis=0).astype(block.dtype)
    return gather_rows(partial, axis)


def input_grad_kernel(scaled_ref, gathered_ref, act_ref, inv_ref, out_ref, feature_ref):
    chunks = gathered_ref.shape[0]
    rows = out_ref.shape[1] // chunks
    scaled = scaled_ref[...]
    inverse = inv_ref[...]
    total = jnp.zeros(inverse.shape, jnp.float32)
    for chunk in range(chunks):
        cols = slice(chunk * rows, (chunk + 1) * rows)
        weight = gathered_ref[chunk, :rows, :]
        feature = D ** (-0.5) * lax.dot_general(
            scaled, weight, (((1,), (1,)), ((), ())), preferred_element_type=jnp.float32
        )
        feature_ref[:, cols] = feature
        normed = act_ref[:, cols].astype(jnp.float32) * inverse
        total = total + jnp.sum(feature * normed, axis=1, keepdims=True)
    projected = total / out_ref.shape[1]
    for chunk in range(chunks):
        cols = slice(chunk * rows, (chunk + 1) * rows)
        normed = act_ref[:, cols].astype(jnp.float32) * inverse
        out_ref[:, cols] = (inverse * (feature_ref[:, cols] - normed * projected)).astype(out_ref.dtype)


def input_grad_of(scaled, gathered, activations, inverse):
    tokens, features = activations.shape
    vmem = pl.BlockSpec(memory_space=pltpu.VMEM)
    return pl.pallas_call(
        input_grad_kernel,
        out_shape=jax.ShapeDtypeStruct((tokens, features), jnp.bfloat16),
        in_specs=[vmem, vmem, vmem, vmem],
        out_specs=vmem,
        scratch_shapes=[pltpu.VMEM((tokens, features), jnp.float32)],
        compiler_params=pltpu.CompilerParams(vmem_limit_bytes=48 * 1024 * 1024),
        cost_estimate=pl.CostEstimate(
            flops=2 * tokens * features * scaled.shape[1],
            bytes_accessed=gathered.size * 2 + activations.size * 4 + scaled.size * 2,
            transcendentals=0,
        ),
    )(scaled, gathered, activations, inverse)


def ring_sum_rows(normed_low, kept, axis):
    count = lax.axis_size(axis)
    stations = count // 2
    me = lax.axis_index(axis)
    station = me // 2
    side = me % 2
    features = normed_low.shape[1]
    width = kept.shape[1]
    group = features // stations
    half = width // 2
    ahead = [(i, ((i // 2 + 1) % stations) * 2 + i % 2) for i in range(count)]
    behind = [(i, ((i // 2 - 1) % stations) * 2 + i % 2) for i in range(count)]
    kept_forward = kept[:, :half]
    kept_backward = kept[:, half:]

    def block(index, right):
        start = pl_multiple((index % stations) * group, group)
        piece = lax.dynamic_slice_in_dim(normed_low, start, group, 1)
        return contract_first(piece, right)

    forward = block(station - 1, kept_forward)
    backward = block(station + 1, kept_backward)
    for step in range(stations - 1):
        forward = lax.ppermute(forward.astype(jnp.bfloat16), axis, ahead).astype(jnp.float32)
        backward = lax.ppermute(backward.astype(jnp.bfloat16), axis, behind).astype(jnp.float32)
        forward = forward + block(station - step - 2, kept_forward)
        backward = backward + block(station + step + 2, kept_backward)
    return jnp.concatenate([forward, backward], axis=1)


def pair_sum_rows(combined, axis):
    count = lax.axis_size(axis)
    side = lax.axis_index(axis) % 2
    rows = combined.shape[0] // 2
    mine = lax.dynamic_slice_in_dim(combined, side * rows, rows, 0)
    theirs = lax.dynamic_slice_in_dim(combined, (1 - side) * rows, rows, 0)
    partner = [(i, i ^ 1) for i in range(count)]
    received = lax.ppermute(theirs.astype(jnp.bfloat16), axis, partner).astype(jnp.float32)
    return mine + received


def pl_multiple(value, step):
    return (value // step) * step


def per_device(
    activations,
    cotangent,
    labels,
    local_weight,
    first_moment,
    second_moment,
    anchor_weight,
    outer_state,
):
    width_scale = D ** (-0.5)
    weight_shard = local_weight[0]
    weight_low = weight_shard.astype(jnp.bfloat16)
    answer = (labels >= 0).astype(jnp.float32)
    rows, width = weight_low.shape
    tokens = cotangent.shape[0]
    flags = jnp.zeros((16, width), jnp.bfloat16).at[0, :tokens].set(answer.astype(jnp.bfloat16))
    packed = jnp.concatenate([weight_low, flags], axis=0)
    gathered = lax.all_gather(packed, "fsdp", axis=0, tiled=False)
    values = activations.astype(jnp.float32)
    inverse = lax.rsqrt(jnp.mean(values * values, axis=1, keepdims=True) + norm_eps)
    normed = values * inverse
    normed_low = normed.astype(jnp.bfloat16)
    kept = (cotangent.astype(jnp.float32) * answer[:, None]).astype(jnp.bfloat16)
    combined = ring_sum_rows(normed_low, kept, "fsdp")
    gathered, combined = lax.optimization_barrier((gathered, combined))
    reduced = pair_sum_rows(combined, "fsdp")
    count = gathered.shape[0]
    all_answer = gathered[:, rows, :tokens].reshape(count * tokens).astype(jnp.float32)
    answers = jnp.sum(all_answer)
    scaled = (cotangent.astype(jnp.float32) * answer[:, None] / answers).astype(jnp.bfloat16)
    input_grad = input_grad_of(scaled, gathered, activations, inverse)
    reduced, input_grad = lax.optimization_barrier((reduced, input_grad))
    gradient = width_scale * reduced / answers
    first = beta_first * first_moment[0].astype(jnp.float32) + (1.0 - beta_first) * gradient
    second = (
        beta_second * second_moment[0].astype(jnp.float32)
        + (1.0 - beta_second) * gradient * gradient
    )
    stepped = weight_shard - inner_rate * (
        first / (jnp.sqrt(second) + adam_eps) + weight_decay * weight_shard
    )
    pseudo_grad = anchor_weight - stepped
    replicas = lax.axis_size("replica")
    average = sum_rows(pseudo_grad.astype(jnp.bfloat16), "replica").astype(jnp.float32) / replicas
    new_state = outer_momentum * outer_state + average
    new_anchor = anchor_weight - outer_rate * (average + outer_momentum * new_state)
    new_first = first.astype(jnp.bfloat16)[None]
    new_second = second.astype(jnp.bfloat16)[None]
    return (input_grad, new_anchor, new_state, new_first, new_second)


def solution(mesh):
    in_specs = (
        P(("replica", "fsdp"), None),
        P(("replica", "fsdp"), None),
        P(("replica", "fsdp")),
        P("replica", "fsdp", None),
        P("replica", "fsdp", None),
        P("replica", "fsdp", None),
        P("fsdp", None),
        P("fsdp", None),
    )
    out_specs = (
        P(("replica", "fsdp"), None),
        P("fsdp", None),
        P("fsdp", None),
        P("replica", "fsdp", None),
        P("replica", "fsdp", None),
    )
    return jax.shard_map(
        per_device, mesh=mesh, in_specs=in_specs, out_specs=out_specs, check_vma=False
    )
```

```python
import jax
import jax.numpy as jnp
from jax import lax
from jax.experimental import pallas as pl
from jax.experimental.pallas import tpu as pltpu
from jax.sharding import PartitionSpec as P

D = 8192


norm_eps = 1e-05
beta_first = 0.9
beta_second = 0.95
adam_eps = 1e-08
weight_decay = 0.1
inner_rate = 0.1
outer_rate = 0.7
outer_momentum = 0.9


def contract_last(left, right):
    return lax.dot_general(
        left, right, (((1,), (1,)), ((), ())), preferred_element_type=jnp.float32
    )


def contract_first(left, right):
    return lax.dot_general(
        left, right, (((0,), (0,)), ((), ())), preferred_element_type=jnp.float32
    )


def gather_rows(block, axis):
    count = lax.axis_size(axis)
    copies = jnp.broadcast_to(block[None], (count,) + block.shape)
    gathered = lax.all_to_all(copies, axis, 0, 0, tiled=True)
    return gathered.reshape((count * block.shape[0],) + block.shape[1:])


def sum_rows(block, axis):
    count = lax.axis_size(axis)
    pieces = block.reshape((count, block.shape[0] // count) + block.shape[1:])
    received = lax.all_to_all(pieces, axis, 0, 0, tiled=True)
    partial = jnp.sum(received.astype(jnp.float32), axis=0).astype(block.dtype)
    return gather_rows(partial, axis)


def input_grad_kernel(scaled_ref, gathered_ref, act_ref, inv_ref, out_ref, feature_ref):
    chunks = gathered_ref.shape[0]
    rows = out_ref.shape[1] // chunks
    scaled = scaled_ref[...]
    inverse = inv_ref[...]
    total = jnp.zeros(inverse.shape, jnp.float32)
    for chunk in range(chunks):
        cols = slice(chunk * rows, (chunk + 1) * rows)
        weight = gathered_ref[chunk, :rows, :]
        feature = D ** (-0.5) * lax.dot_general(
            scaled, weight, (((1,), (1,)), ((), ())), preferred_element_type=jnp.float32
        )
        feature_ref[:, cols] = feature
        normed = act_ref[:, cols].astype(jnp.float32) * inverse
        total = total + jnp.sum(feature * normed, axis=1, keepdims=True)
    projected = total / out_ref.shape[1]
    for chunk in range(chunks):
        cols = slice(chunk * rows, (chunk + 1) * rows)
        normed = act_ref[:, cols].astype(jnp.float32) * inverse
        out_ref[:, cols] = (inverse * (feature_ref[:, cols] - normed * projected)).astype(out_ref.dtype)


def input_grad_of(scaled, gathered, activations, inverse):
    tokens, features = activations.shape
    vmem = pl.BlockSpec(memory_space=pltpu.VMEM)
    return pl.pallas_call(
        input_grad_kernel,
        out_shape=jax.ShapeDtypeStruct((tokens, features), jnp.bfloat16),
        in_specs=[vmem, vmem, vmem, vmem],
        out_specs=vmem,
        scratch_shapes=[pltpu.VMEM((tokens, features), jnp.float32)],
        compiler_params=pltpu.CompilerParams(vmem_limit_bytes=48 * 1024 * 1024),
        cost_estimate=pl.CostEstimate(
            flops=2 * tokens * features * scaled.shape[1],
            bytes_accessed=gathered.size * 2 + activations.size * 4 + scaled.size * 2,
            transcendentals=0,
        ),
    )(scaled, gathered, activations, inverse)


def ring_sum_rows(normed_low, kept, axis):
    count = lax.axis_size(axis)
    stations = count // 2
    me = lax.axis_index(axis)
    station = me // 2
    side = me % 2
    features = normed_low.shape[1]
    width = kept.shape[1]
    group = features // stations
    half = width // 2
    ahead = [(i, ((i // 2 + 1) % stations) * 2 + i % 2) for i in range(count)]
    behind = [(i, ((i // 2 - 1) % stations) * 2 + i % 2) for i in range(count)]
    kept_forward = kept[:, :half]
    kept_backward = kept[:, half:]

    def block(index, right):
        start = pl_multiple((index % stations) * group, group)
        piece = lax.dynamic_slice_in_dim(normed_low, start, group, 1)
        return contract_first(piece, right)

    forward = block(station - 1, kept_forward)
    backward = block(station + 1, kept_backward)
    for step in range(stations - 1):
        forward = lax.ppermute(forward.astype(jnp.bfloat16), axis, ahead).astype(jnp.float32)
        backward = lax.ppermute(backward.astype(jnp.bfloat16), axis, behind).astype(jnp.float32)
        forward = forward + block(station - step - 2, kept_forward)
        backward = backward + block(station + step + 2, kept_backward)
    return jnp.concatenate([forward, backward], axis=1)


def pair_sum_rows(combined, axis):
    count = lax.axis_size(axis)
    side = lax.axis_index(axis) % 2
    rows = combined.shape[0] // 2
    mine = lax.dynamic_slice_in_dim(combined, side * rows, rows, 0)
    theirs = lax.dynamic_slice_in_dim(combined, (1 - side) * rows, rows, 0)
    partner = [(i, i ^ 1) for i in range(count)]
    received = lax.ppermute(theirs.astype(jnp.bfloat16), axis, partner).astype(jnp.float32)
    return mine + received


def pl_multiple(value, step):
    return (value // step) * step


def per_device(
    activations,
    cotangent,
    labels,
    local_weight,
    first_moment,
    second_moment,
    anchor_weight,
    outer_state,
):
    width_scale = D ** (-0.5)
    weight_shard = local_weight[0]
    weight_low = weight_shard.astype(jnp.bfloat16)
    answer = (labels >= 0).astype(jnp.float32)
    rows, width = weight_low.shape
    tokens = cotangent.shape[0]
    flags = jnp.zeros((16, width), jnp.bfloat16).at[0, :tokens].set(answer.astype(jnp.bfloat16))
    packed = jnp.concatenate([weight_low, flags], axis=0)
    gathered = lax.all_gather(packed, "fsdp", axis=0, tiled=False)
    values = activations.astype(jnp.float32)
    inverse = lax.rsqrt(jnp.mean(values * values, axis=1, keepdims=True) + norm_eps)
    normed = values * inverse
    normed_low = normed.astype(jnp.bfloat16)
    kept = (cotangent.astype(jnp.float32) * answer[:, None]).astype(jnp.bfloat16)
    combined = ring_sum_rows(normed_low, kept, "fsdp")
    reduced = pair_sum_rows(combined, "fsdp")
    gathered, reduced = lax.optimization_barrier((gathered, reduced))
    count = gathered.shape[0]
    all_answer = gathered[:, rows, :tokens].reshape(count * tokens).astype(jnp.float32)
    answers = jnp.sum(all_answer)
    scaled = (cotangent.astype(jnp.float32) * answer[:, None] / answers).astype(jnp.bfloat16)
    input_grad = input_grad_of(scaled, gathered, activations, inverse)
    reduced, input_grad = lax.optimization_barrier((reduced, input_grad))
    gradient = width_scale * reduced / answers
    first = beta_first * first_moment[0].astype(jnp.float32) + (1.0 - beta_first) * gradient
    second = (
        beta_second * second_moment[0].astype(jnp.float32)
        + (1.0 - beta_second) * gradient * gradient
    )
    stepped = weight_shard - inner_rate * (
        first / (jnp.sqrt(second) + adam_eps) + weight_decay * weight_shard
    )
    pseudo_grad = anchor_weight - stepped
    replicas = lax.axis_size("replica")
    average = sum_rows(pseudo_grad.astype(jnp.bfloat16), "replica").astype(jnp.float32) / replicas
    new_state = outer_momentum * outer_state + average
    new_anchor = anchor_weight - outer_rate * (average + outer_momentum * new_state)
    new_first = first.astype(jnp.bfloat16)[None]
    new_second = second.astype(jnp.bfloat16)[None]
    return (input_grad, new_anchor, new_state, new_first, new_second)


def solution(mesh):
    in_specs = (
        P(("replica", "fsdp"), None),
        P(("replica", "fsdp"), None),
        P(("replica", "fsdp")),
        P("replica", "fsdp", None),
        P("replica", "fsdp", None),
        P("replica", "fsdp", None),
        P("fsdp", None),
        P("fsdp", None),
    )
    out_specs = (
        P(("replica", "fsdp"), None),
        P("fsdp", None),
        P("fsdp", None),
        P("replica", "fsdp", None),
        P("replica", "fsdp", None),
    )
    return jax.shard_map(
        per_device, mesh=mesh, in_specs=in_specs, out_specs=out_specs, check_vma=False
    )
```

```python
import jax
import jax.numpy as jnp
from jax import lax
from jax.experimental import pallas as pl
from jax.experimental.pallas import tpu as pltpu
from jax.sharding import PartitionSpec as P

D = 8192


norm_eps = 1e-05
beta_first = 0.9
beta_second = 0.95
adam_eps = 1e-08
weight_decay = 0.1
inner_rate = 0.1
outer_rate = 0.7
outer_momentum = 0.9


def contract_last(left, right):
    return lax.dot_general(
        left, right, (((1,), (1,)), ((), ())), preferred_element_type=jnp.float32
    )


def contract_first(left, right):
    return lax.dot_general(
        left, right, (((0,), (0,)), ((), ())), preferred_element_type=jnp.float32
    )


def gather_rows(block, axis):
    count = lax.axis_size(axis)
    copies = jnp.broadcast_to(block[None], (count,) + block.shape)
    gathered = lax.all_to_all(copies, axis, 0, 0, tiled=True)
    return gathered.reshape((count * block.shape[0],) + block.shape[1:])


def sum_rows(block, axis):
    count = lax.axis_size(axis)
    pieces = block.reshape((count, block.shape[0] // count) + block.shape[1:])
    received = lax.all_to_all(pieces, axis, 0, 0, tiled=True)
    partial = jnp.sum(received.astype(jnp.float32), axis=0).astype(block.dtype)
    return gather_rows(partial, axis)


def input_grad_kernel(scaled_ref, gathered_ref, act_ref, inv_ref, out_ref, feature_ref):
    chunks = gathered_ref.shape[0]
    rows = out_ref.shape[1] // chunks
    scaled = scaled_ref[...]
    inverse = inv_ref[...]
    total = jnp.zeros(inverse.shape, jnp.float32)
    for chunk in range(chunks):
        cols = slice(chunk * rows, (chunk + 1) * rows)
        weight = gathered_ref[chunk, :rows, :]
        feature = D ** (-0.5) * lax.dot_general(
            scaled, weight, (((1,), (1,)), ((), ())), preferred_element_type=jnp.float32
        )
        feature_ref[:, cols] = feature
        normed = act_ref[:, cols].astype(jnp.float32) * inverse
        total = total + jnp.sum(feature * normed, axis=1, keepdims=True)
    projected = total / out_ref.shape[1]
    for chunk in range(chunks):
        cols = slice(chunk * rows, (chunk + 1) * rows)
        normed = act_ref[:, cols].astype(jnp.float32) * inverse
        out_ref[:, cols] = (inverse * (feature_ref[:, cols] - normed * projected)).astype(out_ref.dtype)


def input_grad_of(scaled, gathered, activations, inverse):
    tokens, features = activations.shape
    vmem = pl.BlockSpec(memory_space=pltpu.VMEM)
    return pl.pallas_call(
        input_grad_kernel,
        out_shape=jax.ShapeDtypeStruct((tokens, features), jnp.bfloat16),
        in_specs=[vmem, vmem, vmem, vmem],
        out_specs=vmem,
        scratch_shapes=[pltpu.VMEM((tokens, features), jnp.float32)],
        compiler_params=pltpu.CompilerParams(vmem_limit_bytes=48 * 1024 * 1024),
        cost_estimate=pl.CostEstimate(
            flops=2 * tokens * features * scaled.shape[1],
            bytes_accessed=gathered.size * 2 + activations.size * 4 + scaled.size * 2,
            transcendentals=0,
        ),
    )(scaled, gathered, activations, inverse)


def ring_sum_rows(normed_low, kept, axis):
    count = lax.axis_size(axis)
    stations = count // 2
    me = lax.axis_index(axis)
    station = me // 2
    side = me % 2
    features = normed_low.shape[1]
    width = kept.shape[1]
    group = features // stations
    half = width // 2
    ahead = [(i, ((i // 2 + 1) % stations) * 2 + i % 2) for i in range(count)]
    behind = [(i, ((i // 2 - 1) % stations) * 2 + i % 2) for i in range(count)]
    kept_forward = kept[:, :half]
    kept_backward = kept[:, half:]

    def block(index, right):
        start = pl_multiple((index % stations) * group, group)
        piece = lax.dynamic_slice_in_dim(normed_low, start, group, 1)
        return contract_first(piece, right)

    forward = block(station - 1, kept_forward)
    backward = block(station + 1, kept_backward)
    for step in range(stations - 1):
        forward = lax.ppermute(forward.astype(jnp.bfloat16), axis, ahead).astype(jnp.float32)
        backward = lax.ppermute(backward.astype(jnp.bfloat16), axis, behind).astype(jnp.float32)
        forward = forward + block(station - step - 2, kept_forward)
        backward = backward + block(station + step + 2, kept_backward)
    return jnp.concatenate([forward, backward], axis=1)


def pair_sum_rows(combined, axis):
    count = lax.axis_size(axis)
    side = lax.axis_index(axis) % 2
    rows = combined.shape[0] // 2
    mine = lax.dynamic_slice_in_dim(combined, side * rows, rows, 0)
    theirs = lax.dynamic_slice_in_dim(combined, (1 - side) * rows, rows, 0)
    partner = [(i, i ^ 1) for i in range(count)]
    received = lax.ppermute(theirs.astype(jnp.bfloat16), axis, partner).astype(jnp.float32)
    return mine + received


def pl_multiple(value, step):
    return (value // step) * step


def per_device(
    activations,
    cotangent,
    labels,
    local_weight,
    first_moment,
    second_moment,
    anchor_weight,
    outer_state,
):
    width_scale = D ** (-0.5)
    weight_shard = local_weight[0]
    weight_low = weight_shard.astype(jnp.bfloat16)
    answer = (labels >= 0).astype(jnp.float32)
    rows, width = weight_low.shape
    tokens = cotangent.shape[0]
    gathered = lax.all_gather(weight_low, "fsdp", axis=0, tiled=False)
    all_labels = gather_rows(labels, "fsdp")
    values = activations.astype(jnp.float32)
    inverse = lax.rsqrt(jnp.mean(values * values, axis=1, keepdims=True) + norm_eps)
    normed = values * inverse
    normed_low = normed.astype(jnp.bfloat16)
    kept = (cotangent.astype(jnp.float32) * answer[:, None]).astype(jnp.bfloat16)
    combined = ring_sum_rows(normed_low, kept, "fsdp")
    gathered, combined, all_labels = lax.optimization_barrier((gathered, combined, all_labels))
    reduced = pair_sum_rows(combined, "fsdp")
    answers = jnp.sum((all_labels >= 0).astype(jnp.float32))
    scaled = (cotangent.astype(jnp.float32) * answer[:, None] / answers).astype(jnp.bfloat16)
    input_grad = input_grad_of(scaled, gathered, activations, inverse)
    reduced, input_grad = lax.optimization_barrier((reduced, input_grad))
    gradient = width_scale * reduced / answers
    first = beta_first * first_moment[0].astype(jnp.float32) + (1.0 - beta_first) * gradient
    second = (
        beta_second * second_moment[0].astype(jnp.float32)
        + (1.0 - beta_second) * gradient * gradient
    )
    stepped = weight_shard - inner_rate * (
        first / (jnp.sqrt(second) + adam_eps) + weight_decay * weight_shard
    )
    pseudo_grad = anchor_weight - stepped
    replicas = lax.axis_size("replica")
    average = sum_rows(pseudo_grad.astype(jnp.bfloat16), "replica").astype(jnp.float32) / replicas
    new_state = outer_momentum * outer_state + average
    new_anchor = anchor_weight - outer_rate * (average + outer_momentum * new_state)
    new_first = first.astype(jnp.bfloat16)[None]
    new_second = second.astype(jnp.bfloat16)[None]
    return (input_grad, new_anchor, new_state, new_first, new_second)


def solution(mesh):
    in_specs = (
        P(("replica", "fsdp"), None),
        P(("replica", "fsdp"), None),
        P(("replica", "fsdp")),
        P("replica", "fsdp", None),
        P("replica", "fsdp", None),
        P("replica", "fsdp", None),
        P("fsdp", None),
        P("fsdp", None),
    )
    out_specs = (
        P(("replica", "fsdp"), None),
        P("fsdp", None),
        P("fsdp", None),
        P("replica", "fsdp", None),
        P("replica", "fsdp", None),
    )
    return jax.shard_map(
        per_device, mesh=mesh, in_specs=in_specs, out_specs=out_specs, check_vma=False
    )
```
